512 devices in a mesh: pitch: 8 (over z), blk: 64 (over x, y, core).
Axes of the slice: x: 4, y: 8, z: 8, core: 2. Of those that a mesh axis runs over, the one named last changes fastest.
Arguments:
- flux: float32 [128, 64, 45, 128], P('pitch', 'blk'), may hold values from -6 to 6
- pitch_inverse: float32 [64, 128, 128], P('blk', 'pitch')
- span_inverse: float32 [64, 128, 128], P('blk')
- store_old: bfloat16 [8, 64, 128, 45, 128], P('pitch', 'blk'), may hold values from -6 to 6
- send_row: int32 [8, 64, 64], P('pitch', 'blk'), may hold values from 0 to 15
- send_owner: int32 [8, 64, 64], P('pitch', 'blk'), may hold values from 0 to 63, as said below
- send_slot: int32 [8, 64, 64], P('pitch', 'blk'), may hold values from 0 to 127, as said below
- send_count: int32 [8, 64], P('pitch', 'blk'), may hold values from 32 to 64, as said below
Outputs:
- smoothed: float32 [128, 64, 45, 128], P('pitch', 'blk')
- storage: float32 [8, 64, 128, 45, 128], P('pitch', 'blk')
The draws below stay inside these ranges and needn't reach their ends.
Inputs may be any that keep to these rules, and one draw needn't show every extreme that they name: Live entries are the first send_count of each list; in every draw some device has all 64 entries live. `send_owner`: among one device's live entries no owner is named more than 2 times; in every pitch group one owner is named 2 times by the live entries of every device. `send_slot`: within one pitch group, the live entries that name one owner carry distinct slots. `send_row`: the index is r = p * 1 + b on the sending device, with p its local pitch cell and b its local axial cell.
All inputs are finite; a program needn't handle non-finite values.
Results may differ from the reference program's by a relative error of at most 0.0003.
Values sent between devices are 32-bit elements; how exact they have to be, the bound alone decides.
No kernel may reach another device: no remote copies, remote signals or barrier semaphores. Data moves between devices by JAX's collectives and lax.ppermute only.
A program may use at most 64 MiB of HBM per device.

```python
import jax
import jax.numpy as jnp
from jax import lax

FIELDS = 5
INSTANCES = 9
P_SIZE = 128
S = 128
CAP = 2
B_DEV = 1
PD = 16
NB = 64
ROWS_DEV = 16
LIST = 64
STORE = 128
N_PITCH = 8
N_BLK = 64


def decay_table(key, blocks, length, extent, periodic, weight):
    key_fall, key_rough, key_centre = jax.random.split(key, 3)
    positions = jnp.arange(length)
    distance = jnp.abs(positions[:, None] - positions[None, :])
    if periodic:
        distance = jnp.minimum(distance, length - distance)
    falloff = jax.random.uniform(key_fall, (blocks, 1, 1), minval=0.55, maxval=0.85)
    decay = jnp.exp(jnp.log(falloff) * distance.astype(jnp.float32) / extent)
    rough = jax.random.uniform(key_rough, (blocks, length, length), minval=0.5, maxval=1.5)
    centre = jax.random.uniform(key_centre, (blocks, length, 1), minval=0.35, maxval=0.65)
    diagonal = centre * jnp.eye(length, dtype=jnp.float32)
    return (weight / extent * rough * decay + diagonal).astype(jnp.float32)


def draw_pitch_inverse(key, part):
    return decay_table(jax.random.fold_in(key, 3), N_BLK, P_SIZE, P_SIZE // N_PITCH, True, 0.125)


def draw_span_inverse(key, part):
    return decay_table(jax.random.fold_in(key, 5), N_BLK, S, max(S // 4, 1), False, 0.15)


def interface_plan(key):
    base = jax.random.fold_in(key, 11)
    key_count, key_full, key_busy, key_order, key_turn, key_perm = jax.random.split(base, 6)
    pairs = N_BLK * CAP
    list_len = N_BLK * CAP // 2
    least = list_len // 4
    live_count = jax.random.randint(key_count, (N_PITCH, N_BLK), list_len // 2, list_len + 1)
    full_dev = jax.random.randint(key_full, (N_PITCH, 1), 0, N_BLK)
    live_count = jnp.where(jnp.arange(N_BLK)[None, :] == full_dev, list_len, live_count)
    busy = jax.random.randint(key_busy, (N_PITCH, 1), 0, N_BLK)
    scores = jax.random.randint(key_order, (N_PITCH, N_BLK, pairs), 1, 65536)
    pair_owner = jnp.arange(pairs) // CAP
    scores = jnp.where(pair_owner[None, None, :] == busy[:, :, None], 0, scores)
    scores = scores * pairs + jnp.arange(pairs)[None, None, :]
    ordering = jnp.argsort(scores, axis=-1)[:, :, :list_len]
    turn = jax.random.randint(key_turn, (N_PITCH, N_BLK, 1), 0, least)
    spots = jnp.arange(list_len)[None, None, :]
    source = jnp.where(spots < least, (spots + turn) % least, spots)
    chosen = jnp.take_along_axis(ordering, source, axis=-1)
    owner = chosen // CAP
    matches = (owner[..., None] == jnp.arange(N_BLK)[None, None, None, :]).astype(jnp.int32)
    rank = jnp.sum(jnp.cumsum(matches, axis=2) * matches, axis=-1) - 1

    def one_perm(number):
        return jax.random.permutation(jax.random.fold_in(key_perm, number), pairs)
    perms = jax.vmap(one_perm)(jnp.arange(N_PITCH * N_BLK))
    sender = jnp.arange(N_BLK)[None, :, None]
    group = jnp.arange(N_PITCH)[:, None, None]
    flat_index = (group * N_BLK + owner) * pairs + sender * CAP + rank
    slot = perms.reshape(-1)[flat_index]
    return (live_count.astype(jnp.int32), owner.astype(jnp.int32), slot.astype(jnp.int32))


def draw_send_count(key, part):
    return interface_plan(key)[0]


def draw_send_owner(key, part):
    return interface_plan(key)[1]


def draw_send_slot(key, part):
    return interface_plan(key)[2]


def with_ends(array, rng, smallest, largest):
    longest = array.shape.index(max(array.shape))
    spots = []
    for shift in (0, 1):
        where = [jax.random.randint(jax.random.fold_in(rng, axis), (), 0, length) for axis, length in enumerate(array.shape)]
        where[longest] = (where[longest] + shift) % array.shape[longest]
        spots.append(tuple(where))
    return array.at[spots[0]].set(smallest).at[spots[1]].set(largest)


def levels(stream_key, shape, pieces, low, top_value):
    factor_of, own = 1.0, jax.random.fold_in(stream_key, 6)
    for position, parts in pieces:
        draws = jnp.exp(jax.random.uniform(jax.random.fold_in(own, position), (parts,), jnp.float32, low / len(pieces), top_value / len(pieces)))
        factor_of = factor_of * jnp.repeat(draws, shape[position] // parts).reshape([-1 if axis == position else 1 for axis in range(len(shape))])
    return factor_of


def scatter_about(rng, shape, scale, reach, cuts=(), kind=jnp.bfloat16):
    gain = levels(rng, shape, cuts, -0.22, 0.18) if cuts else 1.0
    values = jax.random.normal(rng, shape, jnp.float32) * scale * gain
    return jnp.minimum(jnp.maximum(values, -reach), reach).astype(kind)


def setup_inputs(seed: int = 0) -> dict:
    seeds = jax.random.split(jax.random.key(seed), 9)
    flux = scatter_about(seeds[0], (P_SIZE, NB, FIELDS * INSTANCES, S), 1.0, 6.0, ((0, 8), (1, 64)), jnp.float32)
    pitch_inverse = draw_pitch_inverse(jax.random.fold_in(seeds[8], 71), 0)
    span_inverse = draw_span_inverse(jax.random.fold_in(seeds[8], 71), 0)
    store_old = scatter_about(seeds[3], (N_PITCH, N_BLK, STORE, FIELDS * INSTANCES, S), 1.0, 6.0, ((0, 8), (1, 64)))
    send_row = with_ends(jax.random.randint(seeds[4], (N_PITCH, N_BLK, LIST), 0, ROWS_DEV), jax.random.fold_in(seeds[4], 1), 0, ROWS_DEV - 1).astype(jnp.int32)
    send_owner = draw_send_owner(jax.random.fold_in(seeds[8], 71), 0)
    send_slot = draw_send_slot(jax.random.fold_in(seeds[8], 71), 0)
    send_count = draw_send_count(jax.random.fold_in(seeds[8], 71), 0)
    return dict(flux=flux, pitch_inverse=pitch_inverse, span_inverse=span_inverse, store_old=store_old, send_row=send_row, send_owner=send_owner, send_slot=send_slot, send_count=send_count)


def reference(flux, pitch_inverse, span_inverse, store_old, send_row, send_owner, send_slot, send_count):
    highest = lax.Precision.HIGHEST
    padded = jnp.pad(flux, ((0, 0), (1, 1), (0, 0), (0, 0)))
    residual = 0.25 * padded[:, 2:] - 0.75 * padded[:, :-2] + 0.5 * flux
    grouped = residual.reshape(P_SIZE, N_BLK, -1)
    pitch_smoothed = jnp.einsum("dpk,kdx->pdx", pitch_inverse, grouped, precision=highest)
    pitch_smoothed = pitch_smoothed.reshape(P_SIZE, N_BLK, B_DEV, FIELDS * INSTANCES, S)
    smoothed = jnp.einsum("pdbqs,dts->pdbqt", pitch_smoothed, span_inverse, precision=highest)
    smoothed = smoothed.reshape(flux.shape)
    line_index = send_row.astype(jnp.int32)
    group_ids = jnp.arange(N_PITCH).astype(jnp.int32)[:, None, None]
    block_ids = jnp.arange(N_BLK).astype(jnp.int32)[None, :, None]
    pitch_at = group_ids * PD + line_index // B_DEV
    axial_at = block_ids * B_DEV + line_index % B_DEV
    line_rows = smoothed[pitch_at, axial_at]
    is_live = jnp.arange(LIST).astype(jnp.int32)[None, None, :] < send_count.astype(jnp.int32)[:, :, None]
    target = (group_ids * N_BLK + send_owner.astype(jnp.int32)) * STORE + send_slot.astype(jnp.int32)
    target = jnp.where(is_live, target, N_PITCH * N_BLK * STORE).astype(jnp.int32)
    storage = store_old.astype(jnp.float32).reshape(-1, FIELDS * INSTANCES, S)
    storage = storage.at[target.reshape(-1)].set(line_rows.reshape(-1, FIELDS * INSTANCES, S), mode="drop")
    return smoothed, storage.reshape(store_old.shape)
```

```python
import jax
import jax.numpy as jnp
from jax import lax
from jax.sharding import PartitionSpec as P

CAP = 2


def with_halo(block, axis, dim):
    count = lax.axis_size(axis)
    forward = [(i, i + 1) for i in range(count - 1)]
    backward = [(target, source) for source, target in forward]
    low = lax.ppermute(block, axis, forward)
    high = lax.ppermute(block, axis, backward)
    return low, high


def entry_ranks(owner):
    entries = owner.shape[-1]
    same = owner[..., :, None] == owner[..., None, :]
    earlier = jnp.arange(entries)[None, :] < jnp.arange(entries)[:, None]
    return jnp.sum(same & earlier, axis=-1).astype(jnp.int32)


def local(
    flux, pitch_inverse, span_inverse, store_old, send_row, send_owner, send_slot, send_count
):
    highest = lax.Precision.HIGHEST
    n_pitch = lax.axis_size("pitch")
    n_blk = lax.axis_size("blk")
    me = lax.axis_index("blk")
    pitch_local, axial_local, components, span_cells = flux.shape
    entries = send_owner.shape[2]
    slot_total = store_old.shape[2]

    plan = jnp.concatenate([send_owner[0, 0], send_slot[0, 0], send_count[0]], axis=0)
    plans = lax.all_gather(plan, "blk", axis=0, tiled=False)
    pinv_full = lax.all_gather(pitch_inverse[0], "pitch", axis=0, tiled=True)

    low, high = with_halo(flux, "blk", 1)
    residual = 0.25 * high - 0.75 * low + 0.5 * flux
    padded_q = -(-components // n_pitch) * n_pitch
    chunk_q = padded_q // n_pitch
    res = residual.reshape(pitch_local, components, span_cells)
    res = jnp.pad(res, ((0, 0), (0, padded_q - components), (0, 0)))
    spanned = jnp.einsum("pqs,ts->pqt", res, span_inverse[0], precision=highest)
    chunks = spanned.reshape(pitch_local, n_pitch, chunk_q * span_cells).transpose(1, 0, 2)
    gathered = lax.all_to_all(chunks, "pitch", 0, 0, tiled=True)
    gathered = gathered.reshape(n_pitch * pitch_local, chunk_q * span_cells)
    mixed = jnp.dot(pinv_full, gathered, precision=highest)
    back = lax.all_to_all(
        mixed.reshape(n_pitch, pitch_local, chunk_q * span_cells), "pitch", 0, 0, tiled=True
    )
    smoothed = (
        back.reshape(n_pitch, pitch_local, chunk_q, span_cells)
        .transpose(1, 0, 2, 3)
        .reshape(pitch_local, padded_q, span_cells)[:, :components]
    )

    rows = smoothed.reshape(pitch_local * axial_local, components * span_cells)
    my_owner = send_owner[0, 0]
    live = jnp.arange(entries, dtype=jnp.int32) < send_count[0, 0]
    target = jnp.where(live, my_owner * CAP + entry_ranks(my_owner), -1)
    slot_ids = jnp.arange(n_blk * CAP, dtype=jnp.int32)
    row_ids = jnp.arange(pitch_local * axial_local, dtype=jnp.int32)
    select_out = jnp.any(
        (target[None, :, None] == slot_ids[:, None, None])
        & (send_row[0, 0][None, :, None] == row_ids[None, None, :]),
        axis=1,
    ).astype(jnp.float32)
    outgoing = jnp.dot(select_out, rows, precision=highest)
    arrived = lax.all_to_all(
        outgoing.reshape(n_blk * CAP, components, span_cells), "blk", 0, 0, tiled=True
    )

    owners_all = plans[:, :entries]
    slots_all = plans[:, entries : 2 * entries]
    counts_all = plans[:, 2 * entries]
    ranks_all = entry_ranks(owners_all)
    hit = (jnp.arange(entries, dtype=jnp.int32)[None, :] < counts_all[:, None]) & (
        owners_all == me
    )
    slot_of = jnp.stack(
        [jnp.sum(jnp.where(hit & (ranks_all == c), slots_all + 1, 0), axis=1) - 1 for c in range(CAP)],
        axis=1,
    ).reshape(n_blk * CAP)
    select_in = slot_of[None, :] == jnp.arange(slot_total, dtype=jnp.int32)[:, None]
    filled = jnp.any(select_in, axis=1)
    incoming = jnp.dot(
        select_in.astype(jnp.float32),
        arrived.reshape(n_blk * CAP, components * span_cells),
        precision=highest,
    ).reshape(slot_total, components, span_cells)
    storage = jnp.where(filled[:, None, None], incoming, store_old[0, 0].astype(jnp.float32))
    return (smoothed.reshape(flux.shape), storage[None, None])


def solution(mesh):
    return jax.shard_map(
        local,
        mesh=mesh,
        in_specs=(
            P("pitch", "blk", None, None),
            P("blk", "pitch", None),
            P("blk", None, None),
            P("pitch", "blk", None, None, None),
            P("pitch", "blk", None),
            P("pitch", "blk", None),
            P("pitch", "blk", None),
            P("pitch", "blk"),
        ),
        out_specs=(P("pitch", "blk", None, None), P("pitch", "blk", None, None, None)),
        check_vma=False,
    )
```

```python
import jax
import jax.numpy as jnp
from jax import lax
from jax.sharding import PartitionSpec as P

CAP = 2


def with_halo(block, axis, dim):
    count = lax.axis_size(axis)
    forward = [(i, i + 1) for i in range(count - 1)]
    backward = [(target, source) for source, target in forward]
    low = lax.ppermute(block, axis, forward)
    high = lax.ppermute(block, axis, backward)
    return low, high


def entry_ranks(owner):
    entries = owner.shape[-1]
    same = owner[..., :, None] == owner[..., None, :]
    earlier = jnp.arange(entries)[None, :] < jnp.arange(entries)[:, None]
    return jnp.sum(same & earlier, axis=-1).astype(jnp.int32)


def local(
    flux, pitch_inverse, span_inverse, store_old, send_row, send_owner, send_slot, send_count
):
    highest = lax.Precision.HIGHEST
    n_pitch = lax.axis_size("pitch")
    n_blk = lax.axis_size("blk")
    pitch_local, axial_local, components, span_cells = flux.shape
    entries = send_owner.shape[2]
    slot_total = store_old.shape[2]

    low, high = with_halo(flux, "blk", 1)
    residual = 0.25 * high - 0.75 * low + 0.5 * flux
    padded_q = -(-components // n_pitch) * n_pitch
    chunk_q = padded_q // n_pitch
    width = chunk_q * span_cells
    res = residual.reshape(pitch_local, components, span_cells)
    res = jnp.pad(res, ((0, 0), (0, padded_q - components), (0, 0)))
    spanned = jnp.einsum("pqs,ts->pqt", res, span_inverse[0], precision=highest)
    chunks = spanned.reshape(pitch_local, n_pitch, width).transpose(1, 0, 2)
    pinv_rows = jnp.broadcast_to(pitch_inverse[0][None], (n_pitch,) + pitch_inverse.shape[1:])
    chunks = jnp.concatenate([chunks, pinv_rows], axis=2)
    gathered = lax.all_to_all(chunks, "pitch", 0, 0, tiled=True)
    gathered = gathered.reshape(n_pitch * pitch_local, width + pitch_inverse.shape[2])
    pinv_full = gathered[:, width:]
    mixed = jnp.dot(pinv_full, gathered[:, :width], precision=highest)
    back = lax.all_to_all(mixed.reshape(n_pitch, pitch_local, width), "pitch", 0, 0, tiled=True)
    smoothed = (
        back.reshape(n_pitch, pitch_local, chunk_q, span_cells)
        .transpose(1, 0, 2, 3)
        .reshape(pitch_local, padded_q, span_cells)[:, :components]
    )

    rows = smoothed.reshape(pitch_local * axial_local, components * span_cells)
    my_owner = send_owner[0, 0]
    live = jnp.arange(entries, dtype=jnp.int32) < send_count[0, 0]
    target = jnp.where(live, my_owner * CAP + entry_ranks(my_owner), -1)
    slot_ids = jnp.arange(n_blk * CAP, dtype=jnp.int32)
    row_ids = jnp.arange(pitch_local * axial_local, dtype=jnp.int32)
    hits = target[None, :] == slot_ids[:, None]
    select_out = jnp.any(
        hits[:, :, None] & (send_row[0, 0][None, :, None] == row_ids[None, None, :]), axis=1
    ).astype(jnp.float32)
    tag = jnp.sum(jnp.where(hits, send_slot[0, 0][None, :] + 1, 0), axis=1) - 1
    outgoing = jnp.dot(select_out, rows, precision=highest).reshape(
        n_blk * CAP, components, span_cells
    )
    tag_row = jnp.broadcast_to(tag.astype(jnp.float32)[:, None, None], (n_blk * CAP, 1, span_cells))
    outgoing = jnp.concatenate([outgoing, tag_row], axis=1)
    arrived = lax.all_to_all(outgoing, "blk", 0, 0, tiled=True)

    arrived_slot = arrived[:, components, 0].astype(jnp.int32)
    select_in = arrived_slot[None, :] == jnp.arange(slot_total, dtype=jnp.int32)[:, None]
    filled = jnp.any(select_in, axis=1)
    incoming = jnp.dot(
        select_in.astype(jnp.float32),
        arrived[:, :components].reshape(n_blk * CAP, components * span_cells),
        precision=highest,
    ).reshape(slot_total, components, span_cells)
    storage = jnp.where(filled[:, None, None], incoming, store_old[0, 0].astype(jnp.float32))
    return (smoothed.reshape(flux.shape), storage[None, None])


def solution(mesh):
    return jax.shard_map(
        local,
        mesh=mesh,
        in_specs=(
            P("pitch", "blk", None, None),
            P("blk", "pitch", None),
            P("blk", None, None),
            P("pitch", "blk", None, None, None),
            P("pitch", "blk", None),
            P("pitch", "blk", None),
            P("pitch", "blk", None),
            P("pitch", "blk"),
        ),
        out_specs=(P("pitch", "blk", None, None), P("pitch", "blk", None, None, None)),
        check_vma=False,
    )
```

```python
import jax
import jax.numpy as jnp
from jax import lax
from jax.sharding import PartitionSpec as P

CAP = 2


def with_halo(block, axis, dim):
    count = lax.axis_size(axis)
    forward = [(i, i + 1) for i in range(count - 1)]
    backward = [(target, source) for source, target in forward]
    low = lax.ppermute(block, axis, forward)
    high = lax.ppermute(block, axis, backward)
    return low, high


def entry_ranks(owner):
    entries = owner.shape[-1]
    same = owner[..., :, None] == owner[..., None, :]
    earlier = jnp.arange(entries)[None, :] < jnp.arange(entries)[:, None]
    return jnp.sum(same & earlier, axis=-1).astype(jnp.int32)


def local(
    flux, pitch_inverse, span_inverse, store_old, send_row, send_owner, send_slot, send_count
):
    highest = lax.Precision.HIGHEST
    n_pitch = lax.axis_size("pitch")
    n_blk = lax.axis_size("blk")
    pitch_local, axial_local, components, span_cells = flux.shape
    entries = send_owner.shape[2]
    slot_total = store_old.shape[2]

    low, high = with_halo(flux, "blk", 1)
    residual = 0.25 * high - 0.75 * low + 0.5 * flux
    res = residual.reshape(pitch_local, components, span_cells)
    spanned_all = jnp.einsum("pqs,ts->pqt", res, span_inverse[0], precision=highest)

    my_owner = send_owner[0, 0]
    live = jnp.arange(entries, dtype=jnp.int32) < send_count[0, 0]
    target = jnp.where(live, my_owner * CAP + entry_ranks(my_owner), -1)
    slot_ids = jnp.arange(n_blk * CAP, dtype=jnp.int32)
    row_ids = jnp.arange(pitch_local * axial_local, dtype=jnp.int32)
    hits = target[None, :] == slot_ids[:, None]
    select_out = jnp.any(
        hits[:, :, None] & (send_row[0, 0][None, :, None] == row_ids[None, None, :]), axis=1
    ).astype(jnp.float32)
    tag = jnp.sum(jnp.where(hits, send_slot[0, 0][None, :] + 1, 0), axis=1) - 1
    tag_row = jnp.broadcast_to(tag.astype(jnp.float32)[:, None, None], (n_blk * CAP, 1, span_cells))

    halves = 2
    per_chunk = -(-components // (halves * n_pitch))
    pinv_full = None
    smoothed_parts, arrived_parts = [], []
    for half in range(halves):
        q0 = half * per_chunk * n_pitch
        q1 = min(components, q0 + per_chunk * n_pitch)
        width = per_chunk * span_cells
        part = spanned_all[:, q0:q1]
        part = jnp.pad(part, ((0, 0), (0, per_chunk * n_pitch - (q1 - q0)), (0, 0)))
        chunks = part.reshape(pitch_local, n_pitch, width).transpose(1, 0, 2)
        if pinv_full is None:
            pinv_rows = jnp.broadcast_to(
                pitch_inverse[0][None], (n_pitch,) + pitch_inverse.shape[1:]
            )
            chunks = jnp.concatenate([chunks, pinv_rows], axis=2)
        gathered = lax.all_to_all(chunks, "pitch", 0, 0, tiled=True)
        gathered = gathered.reshape(n_pitch * pitch_local, gathered.shape[2])
        if pinv_full is None:
            pinv_full = gathered[:, width:]
        mixed = jnp.dot(pinv_full, gathered[:, :width], precision=highest)
        back = lax.all_to_all(
            mixed.reshape(n_pitch, pitch_local, width), "pitch", 0, 0, tiled=True
        )
        smooth_part = (
            back.reshape(n_pitch, pitch_local, per_chunk, span_cells)
            .transpose(1, 0, 2, 3)
            .reshape(pitch_local, per_chunk * n_pitch, span_cells)[:, : q1 - q0]
        )
        smoothed_parts.append(smooth_part)
        outgoing = jnp.dot(
            select_out, smooth_part.reshape(pitch_local, (q1 - q0) * span_cells), precision=highest
        ).reshape(n_blk * CAP, q1 - q0, span_cells)
        if half == 0:
            outgoing = jnp.concatenate([outgoing, tag_row], axis=1)
        arrived_parts.append(lax.all_to_all(outgoing, "blk", 0, 0, tiled=True))

    smoothed = jnp.concatenate(smoothed_parts, axis=1)
    first = arrived_parts[0]
    head_q = first.shape[1] - 1
    arrived_slot = first[:, head_q, 0].astype(jnp.int32)
    arrived = jnp.concatenate([first[:, :head_q]] + arrived_parts[1:], axis=1)
    select_in = arrived_slot[None, :] == jnp.arange(slot_total, dtype=jnp.int32)[:, None]
    filled = jnp.any(select_in, axis=1)
    incoming = jnp.dot(
        select_in.astype(jnp.float32),
        arrived.reshape(n_blk * CAP, components * span_cells),
        precision=highest,
    ).reshape(slot_total, components, span_cells)
    storage = jnp.where(filled[:, None, None], incoming, store_old[0, 0].astype(jnp.float32))
    return (smoothed.reshape(flux.shape), storage[None, None])


def solution(mesh):
    return jax.shard_map(
        local,
        mesh=mesh,
        in_specs=(
            P("pitch", "blk", None, None),
            P("blk", "pitch", None),
            P("blk", None, None),
            P("pitch", "blk", None, None, None),
            P("pitch", "blk", None),
            P("pitch", "blk", None),
            P("pitch", "blk", None),
            P("pitch", "blk"),
        ),
        out_specs=(P("pitch", "blk", None, None), P("pitch", "blk", None, None, None)),
        check_vma=False,
    )
```

```python
import jax
import jax.numpy as jnp
from jax import lax
from jax.sharding import PartitionSpec as P

CAP = 2


def with_halo(block, axis, dim):
    count = lax.axis_size(axis)
    forward = [(i, i + 1) for i in range(count - 1)]
    backward = [(target, source) for source, target in forward]
    low = lax.ppermute(block, axis, forward)
    high = lax.ppermute(block, axis, backward)
    return low, high


def entry_ranks(owner):
    entries = owner.shape[-1]
    same = owner[..., :, None] == owner[..., None, :]
    earlier = jnp.arange(entries)[None, :] < jnp.arange(entries)[:, None]
    return jnp.sum(same & earlier, axis=-1).astype(jnp.int32)


def local(
    flux, pitch_inverse, span_inverse, store_old, send_row, send_owner, send_slot, send_count
):
    highest = lax.Precision.HIGHEST
    n_pitch = lax.axis_size("pitch")
    n_blk = lax.axis_size("blk")
    pitch_local, axial_local, components, span_cells = flux.shape
    entries = send_owner.shape[2]
    slot_total = store_old.shape[2]

    low, high = with_halo(flux, "blk", 1)
    residual = 0.25 * high - 0.75 * low + 0.5 * flux
    padded_q = -(-components // n_pitch) * n_pitch
    chunk_q = padded_q // n_pitch
    width = chunk_q * span_cells
    res = residual.reshape(pitch_local, components, span_cells)
    res = jnp.pad(res, ((0, 0), (0, padded_q - components), (0, 0)))
    spanned = jnp.einsum("pqs,ts->pqt", res, span_inverse[0], precision=highest)
    chunks = spanned.reshape(pitch_local, n_pitch, width).transpose(1, 0, 2)
    pinv_rows = jnp.broadcast_to(pitch_inverse[0][None], (n_pitch,) + pitch_inverse.shape[1:])
    chunks = jnp.concatenate([chunks, pinv_rows], axis=2)
    gathered = lax.all_to_all(chunks, "pitch", 0, 0, tiled=True)
    gathered = gathered.reshape(n_pitch * pitch_local, width + pitch_inverse.shape[2])
    pinv_full = gathered[:, width:]
    mixed = jnp.dot(pinv_full, gathered[:, :width], precision=highest)
    back = lax.all_to_all(mixed.reshape(n_pitch, pitch_local, width), "pitch", 0, 0, tiled=True)
    smoothed = (
        back.reshape(n_pitch, pitch_local, chunk_q, span_cells)
        .transpose(1, 0, 2, 3)
        .reshape(pitch_local, padded_q, span_cells)[:, :components]
    )

    rows = smoothed.reshape(pitch_local * axial_local, components * span_cells)
    my_owner = send_owner[0, 0]
    live = jnp.arange(entries, dtype=jnp.int32) < send_count[0, 0]
    target = jnp.where(live, my_owner * CAP + entry_ranks(my_owner), -1)
    slot_ids = jnp.arange(n_blk * CAP, dtype=jnp.int32)
    row_ids = jnp.arange(pitch_local * axial_local, dtype=jnp.int32)
    hits = target[None, :] == slot_ids[:, None]
    select_out = jnp.any(
        hits[:, :, None] & (send_row[0, 0][None, :, None] == row_ids[None, None, :]), axis=1
    ).astype(jnp.float32)
    tag = jnp.sum(jnp.where(hits, send_slot[0, 0][None, :] + 1, 0), axis=1) - 1
    rows_ext = jnp.pad(smoothed.transpose(1, 0, 2), ((0, 1), (0, 1), (0, 0)))
    rows_ext = rows_ext.at[components, pitch_local * axial_local].set(1.0)
    select_ext = jnp.concatenate([select_out, tag.astype(jnp.float32)[:, None]], axis=1)
    outgoing = jnp.einsum("qpt,sp->sqt", rows_ext, select_ext, precision=highest).transpose(1, 0, 2)
    arrived = lax.all_to_all(outgoing, "blk", 1, 1, tiled=True)

    arrived_slot = arrived[components, :, 0].astype(jnp.int32)
    select_in = arrived_slot[None, :] == jnp.arange(slot_total, dtype=jnp.int32)[:, None]
    filled = jnp.any(select_in, axis=1)
    incoming = jnp.einsum(
        "si,qit->qst", select_in.astype(jnp.float32), arrived[:components], precision=highest
    )
    old_t = store_old[0, 0].transpose(1, 0, 2).astype(jnp.float32)
    storage = jnp.where(filled[None, :, None], incoming, old_t).transpose(1, 0, 2)
    return (smoothed.reshape(flux.shape), storage[None, None])


def solution(mesh):
    return jax.shard_map(
        local,
        mesh=mesh,
        in_specs=(
            P("pitch", "blk", None, None),
            P("blk", "pitch", None),
            P("blk", None, None),
            P("pitch", "blk", None, None, None),
            P("pitch", "blk", None),
            P("pitch", "blk", None),
            P("pitch", "blk", None),
            P("pitch", "blk"),
        ),
        out_specs=(P("pitch", "blk", None, None), P("pitch", "blk", None, None, None)),
        check_vma=False,
    )
```

```python
import jax
import jax.numpy as jnp
from jax import lax
from jax.sharding import PartitionSpec as P

CAP = 2


def with_halo(block, axis, dim):
    count = lax.axis_size(axis)
    forward = [(i, i + 1) for i in range(count - 1)]
    backward = [(target, source) for source, target in forward]
    low = lax.ppermute(block, axis, forward)
    high = lax.ppermute(block, axis, backward)
    return low, high


def entry_ranks(owner):
    entries = owner.shape[-1]
    same = owner[..., :, None] == owner[..., None, :]
    earlier = jnp.arange(entries)[None, :] < jnp.arange(entries)[:, None]
    return jnp.sum(same & earlier, axis=-1).astype(jnp.int32)


def local(
    flux, pitch_inverse, span_inverse, store_old, send_row, send_owner, send_slot, send_count
):
    highest = lax.Precision.HIGHEST
    n_pitch = lax.axis_size("pitch")
    n_blk = lax.axis_size("blk")
    pitch_local, axial_local, components, span_cells = flux.shape
    entries = send_owner.shape[2]
    slot_total = store_old.shape[2]

    low, high = with_halo(flux, "blk", 1)
    residual = 0.25 * high - 0.75 * low + 0.5 * flux
    chunk_q = -(-components // (2 * n_pitch))
    split_q = chunk_q * n_pitch
    width = chunk_q * span_cells
    res = residual.reshape(pitch_local, components, span_cells)

    rest = res[:, split_q:].reshape(pitch_local, (components - split_q) * span_cells)
    rest_all = lax.all_gather(rest, "pitch", axis=0, tiled=True)
    rest_mixed = jnp.dot(pitch_inverse[0], rest_all, precision=highest)
    rest_smoothed = jnp.einsum(
        "pqs,ts->pqt",
        rest_mixed.reshape(pitch_local, components - split_q, span_cells),
        span_inverse[0],
        precision=highest,
    )

    spanned = jnp.einsum("pqs,ts->pqt", res[:, :split_q], span_inverse[0], precision=highest)
    chunks = spanned.reshape(pitch_local, n_pitch, width).transpose(1, 0, 2)
    pinv_rows = jnp.broadcast_to(pitch_inverse[0][None], (n_pitch,) + pitch_inverse.shape[1:])
    chunks = jnp.concatenate([chunks, pinv_rows], axis=2)
    gathered = lax.all_to_all(chunks, "pitch", 0, 0, tiled=True)
    gathered = gathered.reshape(n_pitch * pitch_local, width + pitch_inverse.shape[2])
    pinv_full = gathered[:, width:]
    mixed = jnp.dot(pinv_full, gathered[:, :width], precision=highest)
    back = lax.all_to_all(mixed.reshape(n_pitch, pitch_local, width), "pitch", 0, 0, tiled=True)
    head_smoothed = (
        back.reshape(n_pitch, pitch_local, chunk_q, span_cells)
        .transpose(1, 0, 2, 3)
        .reshape(pitch_local, split_q, span_cells)
    )
    smoothed = jnp.concatenate([head_smoothed, rest_smoothed], axis=1)

    rows = smoothed.reshape(pitch_local * axial_local, components * span_cells)
    my_owner = send_owner[0, 0]
    live = jnp.arange(entries, dtype=jnp.int32) < send_count[0, 0]
    target = jnp.where(live, my_owner * CAP + entry_ranks(my_owner), -1)
    slot_ids = jnp.arange(n_blk * CAP, dtype=jnp.int32)
    row_ids = jnp.arange(pitch_local * axial_local, dtype=jnp.int32)
    hits = target[None, :] == slot_ids[:, None]
    select_out = jnp.any(
        hits[:, :, None] & (send_row[0, 0][None, :, None] == row_ids[None, None, :]), axis=1
    ).astype(jnp.float32)
    tag = jnp.sum(jnp.where(hits, send_slot[0, 0][None, :] + 1, 0), axis=1) - 1
    rows_ext = jnp.pad(smoothed.transpose(1, 0, 2), ((0, 1), (0, 1), (0, 0)))
    rows_ext = rows_ext.at[components, pitch_local * axial_local].set(1.0)
    select_ext = jnp.concatenate([select_out, tag.astype(jnp.float32)[:, None]], axis=1)
    outgoing = jnp.einsum("qpt,sp->sqt", rows_ext, select_ext, precision=highest).transpose(1, 0, 2)
    arrived = lax.all_to_all(outgoing, "blk", 1, 1, tiled=True)

    arrived_slot = arrived[components, :, 0].astype(jnp.int32)
    select_in = arrived_slot[None, :] == jnp.arange(slot_total, dtype=jnp.int32)[:, None]
    filled = jnp.any(select_in, axis=1)
    incoming = jnp.einsum(
        "si,qit->qst", select_in.astype(jnp.float32), arrived[:components], precision=highest
    )
    old_t = store_old[0, 0].transpose(1, 0, 2).astype(jnp.float32)
    storage = jnp.where(filled[None, :, None], incoming, old_t).transpose(1, 0, 2)
    return (smoothed.reshape(flux.shape), storage[None, None])


def solution(mesh):
    return jax.shard_map(
        local,
        mesh=mesh,
        in_specs=(
            P("pitch", "blk", None, None),
            P("blk", "pitch", None),
            P("blk", None, None),
            P("pitch", "blk", None, None, None),
            P("pitch", "blk", None),
            P("pitch", "blk", None),
            P("pitch", "blk", None),
            P("pitch", "blk"),
        ),
        out_specs=(P("pitch", "blk", None, None), P("pitch", "blk", None, None, None)),
        check_vma=False,
    )
```

```python
import jax
import jax.numpy as jnp
from jax import lax
from jax.sharding import PartitionSpec as P

CAP = 2


def with_halo(block, axis, dim):
    count = lax.axis_size(axis)
    forward = [(i, i + 1) for i in range(count - 1)]
    backward = [(target, source) for source, target in forward]
    low = lax.ppermute(block, axis, forward)
    high = lax.ppermute(block, axis, backward)
    return low, high


def shifted_exchange(blocks, axis):
    count = lax.axis_size(axis)
    me = lax.axis_index(axis)
    received = [lax.dynamic_index_in_dim(blocks, me, 0, keepdims=False)]
    for shift in range(1, count):
        outgoing = lax.dynamic_index_in_dim(blocks, (me + shift) % count, 0, keepdims=False)
        pairs = [(i, (i + shift) % count) for i in range(count)]
        received.append(lax.ppermute(outgoing, axis, pairs))
    stacked = jnp.stack(received, axis=0)
    order = (me - jnp.arange(count, dtype=jnp.int32)) % count
    return jnp.take(stacked, order, axis=0)


def entry_ranks(owner):
    entries = owner.shape[-1]
    same = owner[..., :, None] == owner[..., None, :]
    earlier = jnp.arange(entries)[None, :] < jnp.arange(entries)[:, None]
    return jnp.sum(same & earlier, axis=-1).astype(jnp.int32)


def local(
    flux, pitch_inverse, span_inverse, store_old, send_row, send_owner, send_slot, send_count
):
    highest = lax.Precision.HIGHEST
    n_pitch = lax.axis_size("pitch")
    n_blk = lax.axis_size("blk")
    pitch_local, axial_local, components, span_cells = flux.shape
    entries = send_owner.shape[2]
    slot_total = store_old.shape[2]

    low, high = with_halo(flux, "blk", 1)
    residual = 0.25 * high - 0.75 * low + 0.5 * flux
    padded_q = -(-components // n_pitch) * n_pitch
    chunk_q = padded_q // n_pitch
    width = chunk_q * span_cells
    res = residual.reshape(pitch_local, components, span_cells)
    res = jnp.pad(res, ((0, 0), (0, padded_q - components), (0, 0)))
    spanned = jnp.einsum("pqs,ts->pqt", res, span_inverse[0], precision=highest)
    chunks = spanned.reshape(pitch_local, n_pitch, width).transpose(1, 0, 2)
    pinv_rows = jnp.broadcast_to(pitch_inverse[0][None], (n_pitch,) + pitch_inverse.shape[1:])
    chunks = jnp.concatenate([chunks, pinv_rows], axis=2)
    gathered = shifted_exchange(chunks, "pitch")
    gathered = gathered.reshape(n_pitch * pitch_local, width + pitch_inverse.shape[2])
    pinv_full = gathered[:, width:]
    mixed = jnp.dot(pinv_full, gathered[:, :width], precision=highest)
    back = shifted_exchange(mixed.reshape(n_pitch, pitch_local, width), "pitch")
    smoothed = (
        back.reshape(n_pitch, pitch_local, chunk_q, span_cells)
        .transpose(1, 0, 2, 3)
        .reshape(pitch_local, padded_q, span_cells)[:, :components]
    )

    rows = smoothed.reshape(pitch_local * axial_local, components * span_cells)
    my_owner = send_owner[0, 0]
    live = jnp.arange(entries, dtype=jnp.int32) < send_count[0, 0]
    target = jnp.where(live, my_owner * CAP + entry_ranks(my_owner), -1)
    slot_ids = jnp.arange(n_blk * CAP, dtype=jnp.int32)
    row_ids = jnp.arange(pitch_local * axial_local, dtype=jnp.int32)
    hits = target[None, :] == slot_ids[:, None]
    select_out = jnp.any(
        hits[:, :, None] & (send_row[0, 0][None, :, None] == row_ids[None, None, :]), axis=1
    ).astype(jnp.float32)
    tag = jnp.sum(jnp.where(hits, send_slot[0, 0][None, :] + 1, 0), axis=1) - 1
    rows_ext = jnp.pad(smoothed.transpose(1, 0, 2), ((0, 1), (0, 1), (0, 0)))
    rows_ext = rows_ext.at[components, pitch_local * axial_local].set(1.0)
    select_ext = jnp.concatenate([select_out, tag.astype(jnp.float32)[:, None]], axis=1)
    outgoing = jnp.einsum("qpt,sp->sqt", rows_ext, select_ext, precision=highest).transpose(1, 0, 2)
    arrived = lax.all_to_all(outgoing, "blk", 1, 1, tiled=True)

    arrived_slot = arrived[components, :, 0].astype(jnp.int32)
    select_in = arrived_slot[None, :] == jnp.arange(slot_total, dtype=jnp.int32)[:, None]
    filled = jnp.any(select_in, axis=1)
    incoming = jnp.einsum(
        "si,qit->qst", select_in.astype(jnp.float32), arrived[:components], precision=highest
    )
    old_t = store_old[0, 0].transpose(1, 0, 2).astype(jnp.float32)
    storage = jnp.where(filled[None, :, None], incoming, old_t).transpose(1, 0, 2)
    return (smoothed.reshape(flux.shape), storage[None, None])


def solution(mesh):
    return jax.shard_map(
        local,
        mesh=mesh,
        in_specs=(
            P("pitch", "blk", None, None),
            P("blk", "pitch", None),
            P("blk", None, None),
            P("pitch", "blk", None, None, None),
            P("pitch", "blk", None),
            P("pitch", "blk", None),
            P("pitch", "blk", None),
            P("pitch", "blk"),
        ),
        out_specs=(P("pitch", "blk", None, None), P("pitch", "blk", None, None, None)),
        check_vma=False,
    )
```

```python
import jax
import jax.numpy as jnp
from jax import lax
from jax.sharding import PartitionSpec as P

CAP = 2


def with_halo(block, axis, dim):
    count = lax.axis_size(axis)
    forward = [(i, i + 1) for i in range(count - 1)]
    backward = [(target, source) for source, target in forward]
    low = lax.ppermute(block, axis, forward)
    high = lax.ppermute(block, axis, backward)
    return low, high


def entry_ranks(owner):
    entries = owner.shape[-1]
    same = owner[..., :, None] == owner[..., None, :]
    earlier = jnp.arange(entries)[None, :] < jnp.arange(entries)[:, None]
    return jnp.sum(same & earlier, axis=-1).astype(jnp.int32)


def local(
    flux, pitch_inverse, span_inverse, store_old, send_row, send_owner, send_slot, send_count
):
    highest = lax.Precision.HIGHEST
    n_pitch = lax.axis_size("pitch")
    n_blk = lax.axis_size("blk")
    pitch_local, axial_local, components, span_cells = flux.shape
    entries = send_owner.shape[2]
    slot_total = store_old.shape[2]

    low, high = with_halo(flux, "blk", 1)
    residual = 0.25 * high - 0.75 * low + 0.5 * flux
    padded_q = -(-components // n_pitch) * n_pitch
    chunk_q = padded_q // n_pitch
    width = chunk_q * span_cells
    res = residual.reshape(pitch_local, components, span_cells)
    res = jnp.pad(res, ((0, 0), (0, padded_q - components), (0, 0)))
    spanned = jnp.einsum("pqs,ts->pqt", res, span_inverse[0], precision=highest)
    chunks = spanned.reshape(pitch_local, n_pitch, width).transpose(1, 0, 2)
    pinv_rows = jnp.broadcast_to(pitch_inverse[0][None], (n_pitch,) + pitch_inverse.shape[1:])
    chunks = jnp.concatenate([chunks, pinv_rows], axis=2)
    gathered = lax.all_to_all(chunks, "pitch", 0, 0, tiled=True)
    gathered = gathered.reshape(n_pitch * pitch_local, width + pitch_inverse.shape[2])
    pinv_full = gathered[:, width:]
    mixed = jnp.dot(pinv_full, gathered[:, :width], precision=highest)
    back = lax.all_to_all(mixed.reshape(n_pitch, pitch_local, width), "pitch", 0, 0, tiled=True)
    smoothed = (
        back.reshape(n_pitch, pitch_local, chunk_q, span_cells)
        .transpose(1, 0, 2, 3)
        .reshape(pitch_local, padded_q, span_cells)[:, :components]
    )

    rows = smoothed.reshape(pitch_local * axial_local, components * span_cells)
    my_owner = send_owner[0, 0]
    live = jnp.arange(entries, dtype=jnp.int32) < send_count[0, 0]
    target = jnp.where(live, my_owner * CAP + entry_ranks(my_owner), -1)
    slot_ids = jnp.arange(n_blk * CAP, dtype=jnp.int32)
    row_ids = jnp.arange(pitch_local * axial_local, dtype=jnp.int32)
    hits = target[None, :] == slot_ids[:, None]
    select_out = jnp.any(
        hits[:, :, None] & (send_row[0, 0][None, :, None] == row_ids[None, None, :]), axis=1
    ).astype(jnp.float32)
    tag = jnp.sum(jnp.where(hits, send_slot[0, 0][None, :] + 1, 0), axis=1) - 1
    rows_ext = jnp.pad(smoothed.transpose(1, 0, 2), ((0, 1), (0, 1), (0, 0)))
    rows_ext = rows_ext.at[components, pitch_local * axial_local].set(1.0)
    select_ext = jnp.concatenate([select_out, tag.astype(jnp.float32)[:, None]], axis=1)
    outgoing = jnp.einsum("qpt,sp->sqt", rows_ext, select_ext, precision=highest).transpose(1, 0, 2)
    arrived = lax.all_to_all(outgoing, "blk", 1, 1, tiled=True)

    slot_lanes = jnp.arange(slot_total, dtype=jnp.float32)[None, :]
    select_in = arrived[components] == slot_lanes
    filled = jnp.any(select_in, axis=0)
    incoming = jnp.einsum(
        "is,qit->qst", select_in.astype(jnp.float32), arrived[:components], precision=highest
    )
    old_t = store_old[0, 0].transpose(1, 0, 2).astype(jnp.float32)
    storage = jnp.where(filled[None, :, None], incoming, old_t).transpose(1, 0, 2)
    return (smoothed.reshape(flux.shape), storage[None, None])


def solution(mesh):
    return jax.shard_map(
        local,
        mesh=mesh,
        in_specs=(
            P("pitch", "blk", None, None),
            P("blk", "pitch", None),
            P("blk", None, None),
            P("pitch", "blk", None, None, None),
            P("pitch", "blk", None),
            P("pitch", "blk", None),
            P("pitch", "blk", None),
            P("pitch", "blk"),
        ),
        out_specs=(P("pitch", "blk", None, None), P("pitch", "blk", None, None, None)),
        check_vma=False,
    )
```

```python
import jax
import jax.numpy as jnp
from jax import lax
from jax.sharding import PartitionSpec as P

CAP = 2


def with_halo(block, axis, dim):
    count = lax.axis_size(axis)
    forward = [(i, i + 1) for i in range(count - 1)]
    backward = [(target, source) for source, target in forward]
    low = lax.ppermute(block, axis, forward)
    high = lax.ppermute(block, axis, backward)
    return low, high


def entry_ranks(owner):
    entries = owner.shape[-1]
    same = owner[..., :, None] == owner[..., None, :]
    earlier = jnp.arange(entries)[None, :] < jnp.arange(entries)[:, None]
    return jnp.sum(same & earlier, axis=-1).astype(jnp.int32)


def local(
    flux, pitch_inverse, span_inverse, store_old, send_row, send_owner, send_slot, send_count
):
    highest = lax.Precision.HIGHEST
    n_pitch = lax.axis_size("pitch")
    n_blk = lax.axis_size("blk")
    pitch_local, axial_local, components, span_cells = flux.shape
    entries = send_owner.shape[2]
    slot_total = store_old.shape[2]

    flat = flux.reshape(pitch_local * axial_local * components, span_cells)
    low, high = with_halo(flat, "blk", 0)
    residual = 0.25 * high - 0.75 * low + 0.5 * flat
    padded_q = -(-components // n_pitch) * n_pitch
    chunk_q = padded_q // n_pitch
    width = chunk_q * span_cells
    res = residual.reshape(pitch_local, components, span_cells)
    res = jnp.pad(res, ((0, 0), (0, padded_q - components), (0, 0)))
    spanned = jnp.einsum("pqs,ts->pqt", res, span_inverse[0], precision=highest)
    chunks = spanned.reshape(pitch_local, n_pitch, width).transpose(1, 0, 2)
    pinv_rows = jnp.broadcast_to(pitch_inverse[0][None], (n_pitch,) + pitch_inverse.shape[1:])
    chunks = jnp.concatenate([chunks, pinv_rows], axis=2)
    gathered = lax.all_to_all(chunks, "pitch", 0, 0, tiled=True)
    gathered = gathered.reshape(n_pitch * pitch_local, width + pitch_inverse.shape[2])
    pinv_full = gathered[:, width:]
    mixed = jnp.dot(pinv_full, gathered[:, :width], precision=highest)
    back = lax.all_to_all(mixed.reshape(n_pitch, pitch_local, width), "pitch", 0, 0, tiled=True)
    smoothed = (
        back.reshape(n_pitch, pitch_local, chunk_q, span_cells)
        .transpose(1, 0, 2, 3)
        .reshape(pitch_local, padded_q, span_cells)[:, :components]
    )

    rows = smoothed.reshape(pitch_local * axial_local, components * span_cells)
    my_owner = send_owner[0, 0]
    live = jnp.arange(entries, dtype=jnp.int32) < send_count[0, 0]
    target = jnp.where(live, my_owner * CAP + entry_ranks(my_owner), -1)
    slot_ids = jnp.arange(n_blk * CAP, dtype=jnp.int32)
    row_ids = jnp.arange(pitch_local * axial_local, dtype=jnp.int32)
    hits = target[None, :] == slot_ids[:, None]
    select_out = jnp.any(
        hits[:, :, None] & (send_row[0, 0][None, :, None] == row_ids[None, None, :]), axis=1
    ).astype(jnp.float32)
    tag = jnp.sum(jnp.where(hits, send_slot[0, 0][None, :] + 1, 0), axis=1) - 1
    rows_ext = jnp.pad(smoothed.transpose(1, 0, 2), ((0, 1), (0, 1), (0, 0)))
    rows_ext = rows_ext.at[components, pitch_local * axial_local].set(1.0)
    select_ext = jnp.concatenate([select_out, tag.astype(jnp.float32)[:, None]], axis=1)
    outgoing = jnp.einsum("qpt,sp->sqt", rows_ext, select_ext, precision=highest).transpose(1, 0, 2)
    arrived = lax.all_to_all(outgoing, "blk", 1, 1, tiled=True)

    slot_lanes = jnp.arange(slot_total, dtype=jnp.float32)[None, :]
    select_in = arrived[components] == slot_lanes
    filled = jnp.any(select_in, axis=0)
    incoming = jnp.einsum(
        "is,qit->qst", select_in.astype(jnp.float32), arrived[:components], precision=highest
    )
    old_t = store_old[0, 0].transpose(1, 0, 2).astype(jnp.float32)
    storage = jnp.where(filled[None, :, None], incoming, old_t).transpose(1, 0, 2)
    return (smoothed.reshape(flux.shape), storage[None, None])


def solution(mesh):
    return jax.shard_map(
        local,
        mesh=mesh,
        in_specs=(
            P("pitch", "blk", None, None),
            P("blk", "pitch", None),
            P("blk", None, None),
            P("pitch", "blk", None, None, None),
            P("pitch", "blk", None),
            P("pitch", "blk", None),
            P("pitch", "blk", None),
            P("pitch", "blk"),
        ),
        out_specs=(P("pitch", "blk", None, None), P("pitch", "blk", None, None, None)),
        check_vma=False,
    )
```

```python
import jax
import jax.numpy as jnp
from jax import lax
from jax.sharding import PartitionSpec as P

CAP = 2


def with_halo(block, axis, dim):
    count = lax.axis_size(axis)
    forward = [(i, i + 1) for i in range(count - 1)]
    backward = [(target, source) for source, target in forward]
    low = lax.ppermute(block, axis, forward)
    high = lax.ppermute(block, axis, backward)
    return low, high


def exact_select(spec, select, values):
    hi_f = lax.reduce_precision(values, exponent_bits=8, mantissa_bits=7)
    rest = values - hi_f
    mid_f = lax.reduce_precision(rest, exponent_bits=8, mantissa_bits=7)
    lo_f = lax.reduce_precision(rest - mid_f, exponent_bits=8, mantissa_bits=7)
    select = select.astype(jnp.bfloat16)
    total = None
    for part in (hi_f, mid_f, lo_f):
        term = jnp.einsum(
            spec, select, part.astype(jnp.bfloat16), preferred_element_type=jnp.float32
        )
        total = term if total is None else total + term
    return total


def entry_ranks(owner):
    entries = owner.shape[-1]
    same = owner[..., :, None] == owner[..., None, :]
    earlier = jnp.arange(entries)[None, :] < jnp.arange(entries)[:, None]
    return jnp.sum(same & earlier, axis=-1).astype(jnp.int32)


def local(
    flux, pitch_inverse, span_inverse, store_old, send_row, send_owner, send_slot, send_count
):
    highest = lax.Precision.HIGHEST
    n_pitch = lax.axis_size("pitch")
    n_blk = lax.axis_size("blk")
    pitch_local, axial_local, components, span_cells = flux.shape
    entries = send_owner.shape[2]
    slot_total = store_old.shape[2]

    flat = flux.reshape(pitch_local * axial_local * components, span_cells)
    low, high = with_halo(flat, "blk", 0)
    residual = 0.25 * high - 0.75 * low + 0.5 * flat
    padded_q = -(-components // n_pitch) * n_pitch
    chunk_q = padded_q // n_pitch
    width = chunk_q * span_cells
    res = residual.reshape(pitch_local, components, span_cells)
    res = jnp.pad(res, ((0, 0), (0, padded_q - components), (0, 0)))
    spanned = jnp.einsum("pqs,ts->pqt", res, span_inverse[0], precision=highest)
    chunks = spanned.reshape(pitch_local, n_pitch, width).transpose(1, 0, 2)
    pinv_rows = jnp.broadcast_to(pitch_inverse[0][None], (n_pitch,) + pitch_inverse.shape[1:])
    chunks = jnp.concatenate([chunks, pinv_rows], axis=2)
    gathered = lax.all_to_all(chunks, "pitch", 0, 0, tiled=True)
    gathered = gathered.reshape(n_pitch * pitch_local, width + pitch_inverse.shape[2])
    pinv_full = gathered[:, width:]
    mixed = jnp.dot(pinv_full, gathered[:, :width], precision=highest)
    back = lax.all_to_all(mixed.reshape(n_pitch, pitch_local, width), "pitch", 0, 0, tiled=True)
    smoothed = (
        back.reshape(n_pitch, pitch_local, chunk_q, span_cells)
        .transpose(1, 0, 2, 3)
        .reshape(pitch_local, padded_q, span_cells)[:, :components]
    )

    rows = smoothed.reshape(pitch_local * axial_local, components * span_cells)
    my_owner = send_owner[0, 0]
    live = jnp.arange(entries, dtype=jnp.int32) < send_count[0, 0]
    target = jnp.where(live, my_owner * CAP + entry_ranks(my_owner), -1)
    slot_ids = jnp.arange(n_blk * CAP, dtype=jnp.int32)
    row_ids = jnp.arange(pitch_local * axial_local, dtype=jnp.int32)
    hits = target[None, :] == slot_ids[:, None]
    select_out = jnp.any(
        hits[:, :, None] & (send_row[0, 0][None, :, None] == row_ids[None, None, :]), axis=1
    ).astype(jnp.float32)
    tag = jnp.sum(jnp.where(hits, send_slot[0, 0][None, :] + 1, 0), axis=1) - 1
    rows_ext = jnp.pad(smoothed.transpose(1, 0, 2), ((0, 1), (0, 1), (0, 0)))
    rows_ext = rows_ext.at[components, pitch_local * axial_local].set(1.0)
    select_ext = jnp.concatenate([select_out, tag.astype(jnp.float32)[:, None]], axis=1)
    outgoing = exact_select("sp,qpt->qst", select_ext, rows_ext)
    arrived = lax.all_to_all(outgoing, "blk", 1, 1, tiled=True)

    slot_lanes = jnp.arange(slot_total, dtype=jnp.float32)[None, :]
    select_in = arrived[components] == slot_lanes
    filled = jnp.any(select_in, axis=0)
    incoming = exact_select("is,qit->qst", select_in, arrived[:components])

    old_t = store_old[0, 0].transpose(1, 0, 2).astype(jnp.float32)
    storage = jnp.where(filled[None, :, None], incoming, old_t).transpose(1, 0, 2)
    return (smoothed.reshape(flux.shape), storage[None, None])


def solution(mesh):
    return jax.shard_map(
        local,
        mesh=mesh,
        in_specs=(
            P("pitch", "blk", None, None),
            P("blk", "pitch", None),
            P("blk", None, None),
            P("pitch", "blk", None, None, None),
            P("pitch", "blk", None),
            P("pitch", "blk", None),
            P("pitch", "blk", None),
            P("pitch", "blk"),
        ),
        out_specs=(P("pitch", "blk", None, None), P("pitch", "blk", None, None, None)),
        check_vma=False,
    )
```

```python
import jax
import jax.numpy as jnp
from jax import lax
from jax.sharding import PartitionSpec as P

CAP = 2


def with_halo(block, axis, dim):
    count = lax.axis_size(axis)
    forward = [(i, i + 1) for i in range(count - 1)]
    backward = [(target, source) for source, target in forward]
    low = lax.ppermute(block, axis, forward)
    high = lax.ppermute(block, axis, backward)
    return low, high


def exact_select(spec, select, values):
    hi_f = lax.reduce_precision(values, exponent_bits=8, mantissa_bits=7)
    rest = values - hi_f
    mid_f = lax.reduce_precision(rest, exponent_bits=8, mantissa_bits=7)
    lo_f = lax.reduce_precision(rest - mid_f, exponent_bits=8, mantissa_bits=7)
    select = select.astype(jnp.bfloat16)
    total = None
    for part in (hi_f, mid_f, lo_f):
        term = jnp.einsum(
            spec, select, part.astype(jnp.bfloat16), preferred_element_type=jnp.float32
        )
        total = term if total is None else total + term
    return total


def entry_ranks(owner):
    entries = owner.shape[-1]
    same = owner[..., :, None] == owner[..., None, :]
    earlier = jnp.arange(entries)[None, :] < jnp.arange(entries)[:, None]
    return jnp.sum(same & earlier, axis=-1).astype(jnp.int32)


def local(
    flux, pitch_inverse, span_inverse, store_old, send_row, send_owner, send_slot, send_count
):
    highest = lax.Precision.HIGHEST
    n_pitch = lax.axis_size("pitch")
    n_blk = lax.axis_size("blk")
    pitch_local, axial_local, components, span_cells = flux.shape
    entries = send_owner.shape[2]
    slot_total = store_old.shape[2]

    flat = flux.reshape(pitch_local * axial_local * components, span_cells)
    low, high = with_halo(flat, "blk", 0)
    residual = 0.25 * high - 0.75 * low + 0.5 * flat
    padded_q = -(-components // n_pitch) * n_pitch
    chunk_q = padded_q // n_pitch
    width = chunk_q * span_cells
    res = residual.reshape(pitch_local, components, span_cells)
    res = jnp.pad(res, ((0, 0), (0, padded_q - components), (0, 0)))
    spanned = jnp.einsum("pqs,ts->pqt", res, span_inverse[0], precision=highest)
    chunks = spanned.reshape(pitch_local, n_pitch, width).transpose(1, 0, 2)
    pinv_rows = jnp.broadcast_to(pitch_inverse[0][None], (n_pitch,) + pitch_inverse.shape[1:])
    chunks = jnp.concatenate([chunks, pinv_rows], axis=2)
    gathered = lax.all_to_all(chunks, "pitch", 0, 0, tiled=True)
    gathered = gathered.reshape(n_pitch * pitch_local, width + pitch_inverse.shape[2])
    pinv_full = gathered[:, width:]
    mixed = jnp.dot(pinv_full, gathered[:, :width], precision=highest)
    back = lax.all_to_all(mixed.reshape(n_pitch, pitch_local, width), "pitch", 0, 0, tiled=True)
    smoothed = (
        back.reshape(n_pitch, pitch_local, chunk_q, span_cells)
        .transpose(1, 0, 2, 3)
        .reshape(pitch_local, padded_q, span_cells)[:, :components]
    )

    rows = smoothed.reshape(pitch_local * axial_local, components * span_cells)
    my_owner = send_owner[0, 0]
    live = jnp.arange(entries, dtype=jnp.int32) < send_count[0, 0]
    target = jnp.where(live, my_owner * CAP + entry_ranks(my_owner), -1)
    slot_ids = jnp.arange(n_blk * CAP, dtype=jnp.int32)
    row_ids = jnp.arange(pitch_local * axial_local, dtype=jnp.int32)
    hits = target[None, :] == slot_ids[:, None]
    select_out = jnp.any(
        hits[:, :, None] & (send_row[0, 0][None, :, None] == row_ids[None, None, :]), axis=1
    ).astype(jnp.float32)
    tag = jnp.sum(jnp.where(hits, send_slot[0, 0][None, :] + 1, 0), axis=1) - 1
    rows_ext = jnp.pad(smoothed.transpose(1, 0, 2), ((0, 1), (0, 1), (0, 0)))
    rows_ext = rows_ext.at[components, pitch_local * axial_local].set(1.0)
    select_ext = jnp.concatenate([select_out, tag.astype(jnp.float32)[:, None]], axis=1)
    outgoing = exact_select("sp,qpt->qst", select_ext, rows_ext)
    arrived = lax.all_to_all(outgoing, "blk", 1, 1, tiled=True)

    slot_lanes = jnp.arange(slot_total, dtype=jnp.float32)[None, :]
    select_in = arrived[components] == slot_lanes
    filled = jnp.any(select_in, axis=0)
    incoming = jnp.einsum(
        "is,qit->qst", select_in.astype(jnp.float32), arrived[:components], precision=highest
    )

    old_t = store_old[0, 0].transpose(1, 0, 2).astype(jnp.float32)
    storage = jnp.where(filled[None, :, None], incoming, old_t).transpose(1, 0, 2)
    return (smoothed.reshape(flux.shape), storage[None, None])


def solution(mesh):
    return jax.shard_map(
        local,
        mesh=mesh,
        in_specs=(
            P("pitch", "blk", None, None),
            P("blk", "pitch", None),
            P("blk", None, None),
            P("pitch", "blk", None, None, None),
            P("pitch", "blk", None),
            P("pitch", "blk", None),
            P("pitch", "blk", None),
            P("pitch", "blk"),
        ),
        out_specs=(P("pitch", "blk", None, None), P("pitch", "blk", None, None, None)),
        check_vma=False,
    )
```
